128 devices in a mesh: row: 16 (over z, x), col: 8 (over y, core).
Axes of the slice: x: 4, y: 4, z: 4, core: 2. Of those that a mesh axis runs over, the one named last changes fastest.
Arguments:
- inputs: bfloat16 [2048, 6144], P('col', 'row'), may hold values from -6 to 6
- out_grad: bfloat16 [2048, 6144], P('col', 'row'), may hold values from -6 to 6
- pre_act: bfloat16 [2048, 24576], P('row', 'col'), may hold values from -8 to 8
- w_in: bfloat16 [6144, 24576], P('row', 'col'), may hold values from -0.078125 to 0.078125
- w_out: bfloat16 [24576, 6144], P('col', 'row'), may hold values from -0.0390625 to 0.0390625
Outputs:
- in_grad: bfloat16 [2048, 6144], P('col', 'row')
- w_in_grad: bfloat16 [6144, 24576], P('row', 'col')
- w_out_grad: bfloat16 [24576, 6144], P('col', 'row')
The draws below stay inside these ranges and needn't reach their ends.
All inputs are finite; a program needn't handle non-finite values.
Results may differ from the reference program's by a relative error of at most 0.03.
Values may be sent and summed in bfloat16 or wider, within the bound.
No kernel may reach another device: no remote copies, remote signals or barrier semaphores. Data moves between devices by JAX's collectives and lax.ppermute only.
A program may use at most 128 MiB of HBM per device.

```python
import jax
import jax.numpy as jnp
from jax import lax

D = 6144
FF = 24576
TOKENS = 2048
N_ROW = 16


def with_spikes(drawn, stream_key, source, target, shards_of, factor):
    def block_of(axis_at):
        return (jnp.arange(drawn.shape[axis_at]) // (drawn.shape[axis_at] // shards_of)).reshape((-1,) + (1,) * (drawn.ndim - 1 - axis_at))

    near = jax.random.permutation(stream_key, shards_of)[block_of(target)]
    second = (block_of(target) + shards_of // 2) % shards_of
    return jnp.where((block_of(source) == near) | (block_of(source) == second), factor * drawn, drawn)


def steps_of(stream_key, shape, cuts, low, largest):
    loudness, own = 1.0, jax.random.fold_in(stream_key, 6)
    for dim, blocks in cuts:
        draws = jnp.exp(jax.random.uniform(jax.random.fold_in(own, dim), (blocks,), jnp.float32, low / len(cuts), largest / len(cuts)))
        loudness = loudness * jnp.repeat(draws, shape[dim] // blocks).reshape([-1 if axis == dim else 1 for axis in range(len(shape))])
    return loudness


def scatter_about(stream_key, shape, spread, bound, cuts=(), held_as=jnp.bfloat16):
    drawn = spread * jax.random.normal(stream_key, shape, jnp.float32)
    if cuts:
        drawn = drawn * steps_of(stream_key, shape, cuts, -0.22, 0.18)
    return jnp.clip(drawn, -bound, bound).astype(held_as)


def bell_draw_with(stream_key, dims, width, limit, pieces, heavy, held_as=jnp.bfloat16):
    array = width * jax.random.normal(stream_key, dims, jnp.float32)
    if pieces:
        array = array * steps_of(stream_key, dims, pieces, -0.22, 0.18)
    return jnp.clip(with_spikes(array, jax.random.fold_in(stream_key, 3), *heavy), -limit, limit).astype(held_as)


def setup_inputs(seed: int = 0) -> dict:
    arg_keys = jax.random.split(jax.random.key(seed), 6)
    inputs = scatter_about(arg_keys[0], (TOKENS, D), 1.0, 6.0, ((0, 8), (1, 16)))
    out_grad = bell_draw_with(arg_keys[1], (TOKENS, D), 1.0, 6.0, ((0, 8), (1, 16)), (1, 0, 16, 2.0))
    pre_act = scatter_about(arg_keys[2], (TOKENS, FF), 1.5, 8.0, ((0, 16), (1, 8)))
    w_in = scatter_about(arg_keys[3], (D, FF), D ** -0.5, 0.078125, ((0, 16), (1, 8)))
    w_out = scatter_about(arg_keys[4], (FF, D), FF ** -0.5, 0.0390625, ((0, 8), (1, 16)))
    return dict(inputs=inputs, out_grad=out_grad, pre_act=pre_act, w_in=w_in, w_out=w_out)


def gelu_parts(pre_act):
    value = pre_act.astype(jnp.float32)
    cumul = 0.5 * (1.0 + jax.scipy.special.erf(value * 0.7071067811865476))
    density = jnp.exp(-0.5 * value * value) * 0.3989422804014327
    return value * cumul, cumul + value * density


def reference(inputs, out_grad, pre_act, w_in, w_out):
    value, slope = gelu_parts(pre_act)
    hidden = value.astype(jnp.bfloat16)
    width_block = out_grad.shape[1] // N_ROW
    hidden_grad = jnp.zeros((out_grad.shape[0], w_out.shape[0]), jnp.float32)
    for block_index in range(N_ROW):
        lower = block_index * width_block
        grad_block = out_grad[:, lower:lower + width_block]
        weight_block = w_out[:, lower:lower + width_block]
        partial_sum = jnp.dot(grad_block, weight_block.T, preferred_element_type=jnp.float32).astype(jnp.bfloat16)
        partial_sum = lax.optimization_barrier(partial_sum)
        hidden_grad = hidden_grad + partial_sum.astype(jnp.float32)
    pre_grad = (hidden_grad * slope).astype(jnp.bfloat16)
    w_out_grad = jnp.dot(hidden.T, out_grad, preferred_element_type=jnp.float32).astype(jnp.bfloat16)
    w_in_grad = jnp.dot(inputs.T, pre_grad, preferred_element_type=jnp.float32).astype(jnp.bfloat16)
    in_grad = jnp.dot(pre_grad, w_in.T, preferred_element_type=jnp.float32).astype(jnp.bfloat16)
    return in_grad, w_in_grad, w_out_grad
```

```python
import jax
import jax.numpy as jnp
from jax import lax
from jax.sharding import PartitionSpec as P


def gelu_parts(pre_act):
    value = pre_act.astype(jnp.float32)
    cumul = 0.5 * (1.0 + jax.scipy.special.erf(value * 0.7071067811865476))
    density = jnp.exp(-0.5 * value * value) * 0.3989422804014327
    return (value * cumul, cumul + value * density)


def gather_by_all_to_all(x, axis, n):
    rep = jnp.concatenate([x] * n, axis=0)
    return lax.all_to_all(rep, axis, 0, 0, tiled=True)


def scatter_sum_by_all_to_all(x, axis, n):
    got = lax.all_to_all(x, axis, 0, 0, tiled=True)
    got = got.reshape((n, x.shape[0] // n) + x.shape[1:])
    acc = got[0].astype(jnp.float32)
    for j in range(1, n):
        acc = acc + got[j].astype(jnp.float32)
    return acc


def on_device(inputs, out_grad, pre_act, w_in, w_out):
    n_col = lax.psum(1, "col")
    value, _ = gelu_parts(pre_act)
    hidden_loc, pre_act = lax.optimization_barrier((value.astype(jnp.bfloat16), pre_act))
    hidden_all = lax.all_gather(hidden_loc, "row", axis=0, tiled=True)
    _, slope = gelu_parts(pre_act)
    grad_all = gather_by_all_to_all(out_grad, "col", n_col)
    inputs_all = gather_by_all_to_all(inputs, "col", n_col)
    partial = lax.dot_general(
        grad_all, w_out, (((1,), (1,)), ((), ())), preferred_element_type=jnp.float32
    ).astype(jnp.bfloat16)
    total = lax.psum_scatter(partial, "row", scatter_dimension=0, tiled=True)
    pre_grad_loc = (total.astype(jnp.float32) * slope).astype(jnp.bfloat16)
    pre_grad = lax.all_gather(pre_grad_loc, "row", axis=0, tiled=True)
    w_out_grad = lax.dot_general(
        hidden_all, grad_all, (((0,), (0,)), ((), ())), preferred_element_type=jnp.float32
    ).astype(jnp.bfloat16)
    w_in_grad = lax.dot_general(
        inputs_all, pre_grad, (((0,), (0,)), ((), ())), preferred_element_type=jnp.float32
    ).astype(jnp.bfloat16)
    in_part = lax.dot_general(
        pre_grad, w_in, (((1,), (1,)), ((), ())), preferred_element_type=jnp.float32
    ).astype(jnp.bfloat16)
    in_grad = scatter_sum_by_all_to_all(in_part, "col", n_col).astype(jnp.bfloat16)
    return (in_grad, w_in_grad, w_out_grad)


def solution(mesh):
    in_specs = (P("col", "row"), P("col", "row"), P("row", "col"), P("row", "col"), P("col", "row"))
    out_specs = (P("col", "row"), P("row", "col"), P("col", "row"))
    return jax.shard_map(
        on_device, mesh=mesh, in_specs=in_specs, out_specs=out_specs, check_vma=False
    )
```

```python
import jax
import jax.numpy as jnp
from jax import lax
from jax.sharding import PartitionSpec as P


def gelu_parts(pre_act):
    value = pre_act.astype(jnp.float32)
    cumul = 0.5 * (1.0 + jax.scipy.special.erf(value * 0.7071067811865476))
    density = jnp.exp(-0.5 * value * value) * 0.3989422804014327
    return (value * cumul, cumul + value * density)


def gather_by_all_to_all(x, axis, n):
    rep = jnp.concatenate([x] * n, axis=0)
    return lax.all_to_all(rep, axis, 0, 0, tiled=True)


def scatter_sum_by_all_to_all(x, axis, n):
    got = lax.all_to_all(x, axis, 0, 0, tiled=True)
    got = got.reshape((n, x.shape[0] // n) + x.shape[1:])
    acc = got[0].astype(jnp.float32)
    for j in range(1, n):
        acc = acc + got[j].astype(jnp.float32)
    return acc


def on_device(inputs, out_grad, pre_act, w_in, w_out):
    n_col = lax.psum(1, "col")
    value, _ = gelu_parts(pre_act)
    hidden_loc, pre_act = lax.optimization_barrier((value.astype(jnp.bfloat16), pre_act))
    hidden_all = lax.all_gather(hidden_loc, "row", axis=0, tiled=True)
    _, slope = gelu_parts(pre_act)
    grad_all = gather_by_all_to_all(out_grad, "col", n_col)
    inputs_all = gather_by_all_to_all(inputs, "col", n_col)
    partial = lax.dot_general(
        grad_all, w_out, (((1,), (1,)), ((), ())), preferred_element_type=jnp.float32
    ).astype(jnp.bfloat16)
    partial, hidden_all = lax.optimization_barrier((partial, hidden_all))
    total = lax.psum_scatter(partial, "row", scatter_dimension=0, tiled=True)
    pre_grad_loc = (total.astype(jnp.float32) * slope).astype(jnp.bfloat16)
    w_out_grad = lax.dot_general(
        hidden_all, grad_all, (((0,), (0,)), ((), ())), preferred_element_type=jnp.float32
    ).astype(jnp.bfloat16)
    n_chunk = 2
    width = pre_grad_loc.shape[1] // n_chunk
    w_in_parts, in_part = [], None
    for k in range(n_chunk):
        cols = slice(k * width, (k + 1) * width)
        pre_grad = lax.all_gather(pre_grad_loc[:, cols], "row", axis=0, tiled=True)
        w_in_parts.append(lax.dot_general(
            inputs_all, pre_grad, (((0,), (0,)), ((), ())), preferred_element_type=jnp.float32
        ).astype(jnp.bfloat16))
        term = lax.dot_general(
            pre_grad, w_in[:, cols], (((1,), (1,)), ((), ())), preferred_element_type=jnp.float32
        )
        in_part = term if in_part is None else in_part + term
    w_in_grad = jnp.concatenate(w_in_parts, axis=1)
    in_grad = scatter_sum_by_all_to_all(in_part.astype(jnp.bfloat16), "col", n_col).astype(jnp.bfloat16)
    return (in_grad, w_in_grad, w_out_grad)


def solution(mesh):
    in_specs = (P("col", "row"), P("col", "row"), P("row", "col"), P("row", "col"), P("col", "row"))
    out_specs = (P("col", "row"), P("row", "col"), P("col", "row"))
    return jax.shard_map(
        on_device, mesh=mesh, in_specs=in_specs, out_specs=out_specs, check_vma=False
    )
```

```python
import jax
import jax.numpy as jnp
from jax import lax
from jax.sharding import PartitionSpec as P


def gelu_parts(pre_act):
    value = pre_act.astype(jnp.float32)
    cumul = 0.5 * (1.0 + jax.scipy.special.erf(value * 0.7071067811865476))
    density = jnp.exp(-0.5 * value * value) * 0.3989422804014327
    return (value * cumul, cumul + value * density)


def gather_by_all_to_all(x, axis, n):
    rep = jnp.concatenate([x] * n, axis=0)
    return lax.all_to_all(rep, axis, 0, 0, tiled=True)


def scatter_sum_by_all_to_all(x, axis, n):
    got = lax.all_to_all(x, axis, 0, 0, tiled=True)
    got = got.reshape((n, x.shape[0] // n) + x.shape[1:])
    acc = got[0].astype(jnp.float32)
    for j in range(1, n):
        acc = acc + got[j].astype(jnp.float32)
    return acc


def gather_col_by_permutes(x, n_y):
    n_col = 2 * n_y
    me = lax.axis_index("col")
    pair = [(c, c ^ 1) for c in range(n_col)]
    other = lax.ppermute(x, "col", pair)
    core = me % 2
    both = jnp.where(core == 0, jnp.concatenate([x, other], 0), jnp.concatenate([other, x], 0))
    fwd = [(c, (c + 2) % n_col) for c in range(n_col)]
    bwd = [(c, (c - 2) % n_col) for c in range(n_col)]
    from_prev = lax.ppermute(both, "col", fwd)
    from_next = lax.ppermute(both, "col", bwd)
    blocks = [both, from_next]
    if n_y == 4:
        blocks.append(lax.ppermute(from_prev, "col", fwd))
    blocks.append(from_prev)
    rel = jnp.concatenate(blocks + blocks, axis=0)
    y = me // 2
    rows = both.shape[0] * n_y
    start = (n_y - y) % n_y * both.shape[0]
    return lax.dynamic_slice_in_dim(rel, start, rows, axis=0)


def on_device(inputs, out_grad, pre_act, w_in, w_out):
    n_col = lax.psum(1, "col")
    value, slope = gelu_parts(pre_act)
    hidden_loc = value.astype(jnp.bfloat16)
    grad_all = gather_col_by_permutes(out_grad, n_col // 2)
    inputs_all = gather_by_all_to_all(inputs, "col", n_col)
    partial = lax.dot_general(
        grad_all, w_out, (((1,), (1,)), ((), ())), preferred_element_type=jnp.float32
    ).astype(jnp.bfloat16)
    total = lax.psum_scatter(partial, "row", scatter_dimension=0, tiled=True)
    pre_grad_loc = (total.astype(jnp.float32) * slope).astype(jnp.bfloat16)
    both = lax.all_gather(jnp.stack([pre_grad_loc, hidden_loc]), "row", axis=1, tiled=True)
    pre_grad, hidden_all = both[0], both[1]
    in_part = lax.dot_general(
        pre_grad, w_in, (((1,), (1,)), ((), ())), preferred_element_type=jnp.float32
    ).astype(jnp.bfloat16)
    in_grad = scatter_sum_by_all_to_all(in_part, "col", n_col).astype(jnp.bfloat16)
    w_out_grad = lax.dot_general(
        hidden_all, grad_all, (((0,), (0,)), ((), ())), preferred_element_type=jnp.float32
    ).astype(jnp.bfloat16)
    w_in_grad = lax.dot_general(
        inputs_all, pre_grad, (((0,), (0,)), ((), ())), preferred_element_type=jnp.float32
    ).astype(jnp.bfloat16)
    return (in_grad, w_in_grad, w_out_grad)


def solution(mesh):
    in_specs = (P("col", "row"), P("col", "row"), P("row", "col"), P("row", "col"), P("col", "row"))
    out_specs = (P("col", "row"), P("row", "col"), P("col", "row"))
    return jax.shard_map(
        on_device, mesh=mesh, in_specs=in_specs, out_specs=out_specs, check_vma=False
    )
```

```python
import jax
import jax.numpy as jnp
from jax import lax
from jax.sharding import PartitionSpec as P


def gelu_parts(pre_act):
    value = pre_act.astype(jnp.float32)
    cumul = 0.5 * (1.0 + jax.scipy.special.erf(value * 0.7071067811865476))
    density = jnp.exp(-0.5 * value * value) * 0.3989422804014327
    return (value * cumul, cumul + value * density)


def gather_by_all_to_all(x, axis, n):
    rep = jnp.concatenate([x] * n, axis=0)
    return lax.all_to_all(rep, axis, 0, 0, tiled=True)


def scatter_sum_by_all_to_all(x, axis, n):
    got = lax.all_to_all(x, axis, 0, 0, tiled=True)
    got = got.reshape((n, x.shape[0] // n) + x.shape[1:])
    acc = got[0].astype(jnp.float32)
    for j in range(1, n):
        acc = acc + got[j].astype(jnp.float32)
    return acc


def gather_col_by_permutes(x, n_y):
    n_col = 2 * n_y
    me = lax.axis_index("col")
    pair = [(c, c ^ 1) for c in range(n_col)]
    other = lax.ppermute(x, "col", pair)
    core = me % 2
    both = jnp.where(core == 0, jnp.concatenate([x, other], 0), jnp.concatenate([other, x], 0))
    fwd = [(c, (c + 2) % n_col) for c in range(n_col)]
    bwd = [(c, (c - 2) % n_col) for c in range(n_col)]
    from_prev = lax.ppermute(both, "col", fwd)
    from_next = lax.ppermute(both, "col", bwd)
    blocks = [both, from_next]
    if n_y == 4:
        blocks.append(lax.ppermute(from_prev, "col", fwd))
    blocks.append(from_prev)
    rel = jnp.concatenate(blocks + blocks, axis=0)
    y = me // 2
    rows = both.shape[0] * n_y
    start = (n_y - y) % n_y * both.shape[0]
    return lax.dynamic_slice_in_dim(rel, start, rows, axis=0)


def on_device(inputs, out_grad, pre_act, w_in, w_out):
    n_col = lax.psum(1, "col")
    value, slope = gelu_parts(pre_act)
    hidden_all = lax.all_gather(value.astype(jnp.bfloat16), "row", axis=0, tiled=True)
    grad_all = gather_by_all_to_all(out_grad, "col", n_col)
    inputs_all = gather_by_all_to_all(inputs, "col", n_col)
    partial = lax.dot_general(
        grad_all, w_out, (((1,), (1,)), ((), ())), preferred_element_type=jnp.float32
    ).astype(jnp.bfloat16)
    partial, hidden_all = lax.optimization_barrier((partial, hidden_all))
    total = lax.psum_scatter(partial, "row", scatter_dimension=0, tiled=True)
    w_out_grad = lax.dot_general(
        hidden_all, grad_all, (((0,), (0,)), ((), ())), preferred_element_type=jnp.float32
    ).astype(jnp.bfloat16)
    total, w_out_grad = lax.optimization_barrier((total, w_out_grad))
    pre_grad_loc = (total.astype(jnp.float32) * slope).astype(jnp.bfloat16)
    pre_grad = lax.all_gather(pre_grad_loc, "row", axis=0, tiled=True)
    in_part = lax.dot_general(
        pre_grad, w_in, (((1,), (1,)), ((), ())), preferred_element_type=jnp.float32
    ).astype(jnp.bfloat16)
    in_grad = scatter_sum_by_all_to_all(in_part, "col", n_col).astype(jnp.bfloat16)
    w_in_grad = lax.dot_general(
        inputs_all, pre_grad, (((0,), (0,)), ((), ())), preferred_element_type=jnp.float32
    ).astype(jnp.bfloat16)
    return (in_grad, w_in_grad, w_out_grad)


def solution(mesh):
    in_specs = (P("col", "row"), P("col", "row"), P("row", "col"), P("row", "col"), P("col", "row"))
    out_specs = (P("col", "row"), P("row", "col"), P("col", "row"))
    return jax.shard_map(
        on_device, mesh=mesh, in_specs=in_specs, out_specs=out_specs, check_vma=False
    )
```

```python
import jax
import jax.numpy as jnp
from jax import lax
from jax.sharding import PartitionSpec as P


def gelu_parts(pre_act):
    value = pre_act.astype(jnp.float32)
    cumul = 0.5 * (1.0 + jax.scipy.special.erf(value * 0.7071067811865476))
    density = jnp.exp(-0.5 * value * value) * 0.3989422804014327
    return (value * cumul, cumul + value * density)


def gather_by_all_to_all(x, axis, n):
    rep = jnp.concatenate([x] * n, axis=0)
    return lax.all_to_all(rep, axis, 0, 0, tiled=True)


def scatter_sum_by_all_to_all(x, axis, n):
    got = lax.all_to_all(x, axis, 0, 0, tiled=True)
    got = got.reshape((n, x.shape[0] // n) + x.shape[1:])
    acc = got[0].astype(jnp.float32)
    for j in range(1, n):
        acc = acc + got[j].astype(jnp.float32)
    return acc


def gather_col_by_permutes(x, n_y):
    n_col = 2 * n_y
    me = lax.axis_index("col")
    pair = [(c, c ^ 1) for c in range(n_col)]
    other = lax.ppermute(x, "col", pair)
    core = me % 2
    both = jnp.where(core == 0, jnp.concatenate([x, other], 0), jnp.concatenate([other, x], 0))
    fwd = [(c, (c + 2) % n_col) for c in range(n_col)]
    bwd = [(c, (c - 2) % n_col) for c in range(n_col)]
    from_prev = lax.ppermute(both, "col", fwd)
    from_next = lax.ppermute(both, "col", bwd)
    blocks = [both, from_next]
    if n_y == 4:
        blocks.append(lax.ppermute(from_prev, "col", fwd))
    blocks.append(from_prev)
    rel = jnp.concatenate(blocks + blocks, axis=0)
    y = me // 2
    rows = both.shape[0] * n_y
    start = (n_y - y) % n_y * both.shape[0]
    return lax.dynamic_slice_in_dim(rel, start, rows, axis=0)


def ring_gather(x, fwd, bwd):
    from_prev = lax.ppermute(x, "row", fwd)
    from_next = lax.ppermute(x, "row", bwd)
    h = x.shape[0] // 2
    far = jnp.concatenate(
        [lax.ppermute(from_prev[:h], "row", fwd), lax.ppermute(from_next[h:], "row", bwd)], 0
    )
    return jnp.stack([x, from_next, far, from_prev])


def torus_gather(block, n_z, n_x):
    def perm(dz, dx):
        return [(z * n_x + x, ((z + dz) % n_z) * n_x + (x + dx) % n_x)
                for z in range(n_z) for x in range(n_x)]
    fx, bx, fz, bz = perm(0, 1), perm(0, -1), perm(1, 0), perm(-1, 0)
    w = block.shape[1] // 2
    a = ring_gather(ring_gather(block[:, :w], fx, bx), fz, bz)
    b = ring_gather(ring_gather(block[:, w:], fz, bz), fx, bx)
    return a, b


def on_device(inputs, out_grad, pre_act, w_in, w_out):
    n_col = lax.psum(1, "col")
    value, slope = gelu_parts(pre_act)
    hidden_loc = value.astype(jnp.bfloat16)
    n_z, n_x = 4, 4
    hid_a, hid_b = torus_gather(hidden_loc, n_z, n_x)
    grad_all = gather_by_all_to_all(out_grad, "col", n_col)
    inputs_all = gather_by_all_to_all(inputs, "col", n_col)
    partial = lax.dot_general(
        grad_all, w_out, (((1,), (1,)), ((), ())), preferred_element_type=jnp.float32
    ).astype(jnp.bfloat16)
    total = lax.psum_scatter(partial, "row", scatter_dimension=0, tiled=True)
    me = lax.axis_index("row")
    grad4 = grad_all.reshape((n_z, n_x, -1, grad_all.shape[1]))
    grad_rel = jnp.roll(grad4, (-(me // n_x), -(me % n_x)), axis=(0, 1))
    width = hid_a.shape[-1]
    w_out_a = lax.dot_general(
        hid_a.reshape(-1, width), grad_rel.reshape(-1, grad_all.shape[1]),
        (((0,), (0,)), ((), ())), preferred_element_type=jnp.float32
    )
    w_out_b = lax.dot_general(
        hid_b.reshape(-1, width), jnp.swapaxes(grad_rel, 0, 1).reshape(-1, grad_all.shape[1]),
        (((0,), (0,)), ((), ())), preferred_element_type=jnp.float32
    )
    w_out_grad = jnp.concatenate([w_out_a, w_out_b], axis=0).astype(jnp.bfloat16)
    total, w_out_grad = lax.optimization_barrier((total, w_out_grad))
    pre_grad_loc = (total.astype(jnp.float32) * slope).astype(jnp.bfloat16)
    pre_grad = lax.all_gather(pre_grad_loc, "row", axis=0, tiled=True)
    in_part = lax.dot_general(
        pre_grad, w_in, (((1,), (1,)), ((), ())), preferred_element_type=jnp.float32
    ).astype(jnp.bfloat16)
    in_grad = scatter_sum_by_all_to_all(in_part, "col", n_col).astype(jnp.bfloat16)
    w_in_grad = lax.dot_general(
        inputs_all, pre_grad, (((0,), (0,)), ((), ())), preferred_element_type=jnp.float32
    ).astype(jnp.bfloat16)
    return (in_grad, w_in_grad, w_out_grad)


def solution(mesh):
    in_specs = (P("col", "row"), P("col", "row"), P("row", "col"), P("row", "col"), P("col", "row"))
    out_specs = (P("col", "row"), P("row", "col"), P("col", "row"))
    return jax.shard_map(
        on_device, mesh=mesh, in_specs=in_specs, out_specs=out_specs, check_vma=False
    )
```

```python
import jax
import jax.numpy as jnp
from jax import lax
from jax.sharding import PartitionSpec as P


def gelu_parts(pre_act):
    value = pre_act.astype(jnp.float32)
    cumul = 0.5 * (1.0 + jax.scipy.special.erf(value * 0.7071067811865476))
    density = jnp.exp(-0.5 * value * value) * 0.3989422804014327
    return (value * cumul, cumul + value * density)


def gather_by_all_to_all(x, axis, n):
    rep = jnp.concatenate([x] * n, axis=0)
    return lax.all_to_all(rep, axis, 0, 0, tiled=True)


def scatter_sum_by_all_to_all(x, axis, n):
    got = lax.all_to_all(x, axis, 0, 0, tiled=True)
    got = got.reshape((n, x.shape[0] // n) + x.shape[1:])
    acc = got[0].astype(jnp.float32)
    for j in range(1, n):
        acc = acc + got[j].astype(jnp.float32)
    return acc


def gather_col_by_permutes(x, n_y):
    n_col = 2 * n_y
    me = lax.axis_index("col")
    pair = [(c, c ^ 1) for c in range(n_col)]
    other = lax.ppermute(x, "col", pair)
    core = me % 2
    both = jnp.where(core == 0, jnp.concatenate([x, other], 0), jnp.concatenate([other, x], 0))
    fwd = [(c, (c + 2) % n_col) for c in range(n_col)]
    bwd = [(c, (c - 2) % n_col) for c in range(n_col)]
    from_prev = lax.ppermute(both, "col", fwd)
    from_next = lax.ppermute(both, "col", bwd)
    blocks = [both, from_next]
    if n_y == 4:
        blocks.append(lax.ppermute(from_prev, "col", fwd))
    blocks.append(from_prev)
    rel = jnp.concatenate(blocks + blocks, axis=0)
    y = me // 2
    rows = both.shape[0] * n_y
    start = (n_y - y) % n_y * both.shape[0]
    return lax.dynamic_slice_in_dim(rel, start, rows, axis=0)


def ring_gather(x, fwd, bwd):
    from_prev = lax.ppermute(x, "row", fwd)
    from_next = lax.ppermute(x, "row", bwd)
    h = x.shape[0] // 2
    far = jnp.concatenate(
        [lax.ppermute(from_prev[:h], "row", fwd), lax.ppermute(from_next[h:], "row", bwd)], 0
    )
    return jnp.stack([x, from_next, far, from_prev])


def torus_gather(block, n_z, n_x, after):
    def perm(dz, dx):
        return [(z * n_x + x, ((z + dz) % n_z) * n_x + (x + dx) % n_x)
                for z in range(n_z) for x in range(n_x)]
    fx, bx, fz, bz = perm(0, 1), perm(0, -1), perm(1, 0), perm(-1, 0)
    w = block.shape[1] // 2
    a1 = ring_gather(block[:, :w], fx, bx)
    b1 = ring_gather(block[:, w:], fz, bz)
    a1, b1, after = lax.optimization_barrier((a1, b1, after))
    a = ring_gather(a1, fz, bz)
    b = ring_gather(b1, fx, bx)
    return a, b, after


def on_device(inputs, out_grad, pre_act, w_in, w_out):
    n_col = lax.psum(1, "col")
    value, slope = gelu_parts(pre_act)
    hidden_loc = value.astype(jnp.bfloat16)
    n_z, n_x = 4, 4
    grad_all = gather_by_all_to_all(out_grad, "col", n_col)
    hid_a, hid_b, grad_all = torus_gather(hidden_loc, n_z, n_x, grad_all)
    inputs_all = gather_by_all_to_all(inputs, "col", n_col)
    partial = lax.dot_general(
        grad_all, w_out, (((1,), (1,)), ((), ())), preferred_element_type=jnp.float32
    ).astype(jnp.bfloat16)
    total = lax.psum_scatter(partial, "row", scatter_dimension=0, tiled=True)
    me = lax.axis_index("row")
    grad4 = grad_all.reshape((n_z, n_x, -1, grad_all.shape[1]))
    grad_rel = jnp.roll(grad4, (-(me // n_x), -(me % n_x)), axis=(0, 1))
    width = hid_a.shape[-1]
    w_out_a = lax.dot_general(
        hid_a.reshape(-1, width), grad_rel.reshape(-1, grad_all.shape[1]),
        (((0,), (0,)), ((), ())), preferred_element_type=jnp.float32
    )
    w_out_b = lax.dot_general(
        hid_b.reshape(-1, width), jnp.swapaxes(grad_rel, 0, 1).reshape(-1, grad_all.shape[1]),
        (((0,), (0,)), ((), ())), preferred_element_type=jnp.float32
    )
    w_out_grad = jnp.concatenate([w_out_a, w_out_b], axis=0).astype(jnp.bfloat16)
    total, w_out_grad = lax.optimization_barrier((total, w_out_grad))
    pre_grad_loc = (total.astype(jnp.float32) * slope).astype(jnp.bfloat16)
    pre_grad = lax.all_gather(pre_grad_loc, "row", axis=0, tiled=True)
    in_part = lax.dot_general(
        pre_grad, w_in, (((1,), (1,)), ((), ())), preferred_element_type=jnp.float32
    ).astype(jnp.bfloat16)
    in_grad = scatter_sum_by_all_to_all(in_part, "col", n_col).astype(jnp.bfloat16)
    w_in_grad = lax.dot_general(
        inputs_all, pre_grad, (((0,), (0,)), ((), ())), preferred_element_type=jnp.float32
    ).astype(jnp.bfloat16)
    return (in_grad, w_in_grad, w_out_grad)


def solution(mesh):
    in_specs = (P("col", "row"), P("col", "row"), P("row", "col"), P("row", "col"), P("col", "row"))
    out_specs = (P("col", "row"), P("row", "col"), P("col", "row"))
    return jax.shard_map(
        on_device, mesh=mesh, in_specs=in_specs, out_specs=out_specs, check_vma=False
    )
```

```python
import jax
import jax.numpy as jnp
from jax import lax
from jax.sharding import PartitionSpec as P


def gelu_parts(pre_act):
    value = pre_act.astype(jnp.float32)
    cumul = 0.5 * (1.0 + jax.scipy.special.erf(value * 0.7071067811865476))
    density = jnp.exp(-0.5 * value * value) * 0.3989422804014327
    return (value * cumul, cumul + value * density)


def gather_by_all_to_all(x, axis, n):
    rep = jnp.concatenate([x] * n, axis=0)
    return lax.all_to_all(rep, axis, 0, 0, tiled=True)


def scatter_sum_by_all_to_all(x, axis, n):
    got = lax.all_to_all(x, axis, 0, 0, tiled=True)
    got = got.reshape((n, x.shape[0] // n) + x.shape[1:])
    acc = got[0].astype(jnp.float32)
    for j in range(1, n):
        acc = acc + got[j].astype(jnp.float32)
    return acc


def gather_col_by_permutes(x, n_y):
    n_col = 2 * n_y
    me = lax.axis_index("col")
    pair = [(c, c ^ 1) for c in range(n_col)]
    other = lax.ppermute(x, "col", pair)
    core = me % 2
    both = jnp.where(core == 0, jnp.concatenate([x, other], 0), jnp.concatenate([other, x], 0))
    fwd = [(c, (c + 2) % n_col) for c in range(n_col)]
    bwd = [(c, (c - 2) % n_col) for c in range(n_col)]
    from_prev = lax.ppermute(both, "col", fwd)
    from_next = lax.ppermute(both, "col", bwd)
    blocks = [both, from_next]
    if n_y == 4:
        blocks.append(lax.ppermute(from_prev, "col", fwd))
    blocks.append(from_prev)
    rel = jnp.concatenate(blocks + blocks, axis=0)
    y = me // 2
    rows = both.shape[0] * n_y
    start = (n_y - y) % n_y * both.shape[0]
    return lax.dynamic_slice_in_dim(rel, start, rows, axis=0)


def ring_gather(x, fwd, bwd):
    from_prev = lax.ppermute(x, "row", fwd)
    from_next = lax.ppermute(x, "row", bwd)
    h = x.shape[0] // 2
    far = jnp.concatenate(
        [lax.ppermute(from_prev[:h], "row", fwd), lax.ppermute(from_next[h:], "row", bwd)], 0
    )
    return jnp.stack([x, from_next, far, from_prev])


def torus_gather(block, n_z, n_x, after):
    def perm(dz, dx):
        return [(z * n_x + x, ((z + dz) % n_z) * n_x + (x + dx) % n_x)
                for z in range(n_z) for x in range(n_x)]
    fx, bx, fz, bz = perm(0, 1), perm(0, -1), perm(1, 0), perm(-1, 0)
    w = block.shape[1] // 2
    a1 = ring_gather(block[:, :w], fx, bx)
    b1 = ring_gather(block[:, w:], fz, bz)
    a1, b1, after = lax.optimization_barrier((a1, b1, after))
    a = ring_gather(a1, fz, bz)
    b = ring_gather(b1, fx, bx)
    return a, b, after


def on_device(inputs, out_grad, pre_act, w_in, w_out):
    n_col = lax.psum(1, "col")
    value, slope = gelu_parts(pre_act)
    hidden_loc = value.astype(jnp.bfloat16)
    n_z, n_x = 4, 4
    grad_all = gather_by_all_to_all(out_grad, "col", n_col)
    hid_a, hid_b, grad_all = torus_gather(hidden_loc, n_z, n_x, grad_all)
    inputs_all = gather_by_all_to_all(inputs, "col", n_col)
    partial = lax.dot_general(
        grad_all, w_out, (((1,), (1,)), ((), ())), preferred_element_type=jnp.float32
    ).astype(jnp.bfloat16)
    total = lax.psum_scatter(partial, "row", scatter_dimension=0, tiled=True)
    me = lax.axis_index("row")
    grad4 = grad_all.reshape((n_z, n_x, -1, grad_all.shape[1]))
    grad_rel = jnp.roll(grad4, (-(me // n_x), -(me % n_x)), axis=(0, 1))
    width = hid_a.shape[-1]
    w_out_a = lax.dot_general(
        hid_a.reshape(-1, width), grad_rel.reshape(-1, grad_all.shape[1]),
        (((0,), (0,)), ((), ())), preferred_element_type=jnp.float32
    )
    w_out_b = lax.dot_general(
        hid_b.reshape(-1, width), jnp.swapaxes(grad_rel, 0, 1).reshape(-1, grad_all.shape[1]),
        (((0,), (0,)), ((), ())), preferred_element_type=jnp.float32
    )
    w_out_grad = jnp.concatenate([w_out_a, w_out_b], axis=0).astype(jnp.bfloat16)
    total, w_out_grad = lax.optimization_barrier((total, w_out_grad))
    pre_grad_loc = (total.astype(jnp.float32) * slope).astype(jnp.bfloat16)
    half = pre_grad_loc.shape[1] // 2
    pre_sc = lax.all_gather(pre_grad_loc[:, :half], "row", axis=0, tiled=True)
    pre_a, pre_b, _ = torus_gather(pre_grad_loc[:, half:], n_z, n_x, pre_grad_loc[:1, :1])
    q = pre_a.shape[-1]
    x4 = inputs_all.reshape((n_z, n_x, -1, inputs_all.shape[1]))
    x_rel = jnp.roll(x4, (-(me // n_x), -(me % n_x)), axis=(0, 1))
    d_blk = inputs_all.shape[1]

    def in_term(p, w):
        return lax.dot_general(p, w, (((p.ndim - 1,), (1,)), ((), ())),
                               preferred_element_type=jnp.float32)

    in_part = in_term(pre_sc, w_in[:, :half])
    rel_a = in_term(pre_a, w_in[:, half:half + q])
    rel_b = jnp.swapaxes(in_term(pre_b, w_in[:, half + q:]), 0, 1)
    back = jnp.roll(rel_a + rel_b, (me // n_x, me % n_x), axis=(0, 1))
    in_part = (in_part + back.reshape(in_part.shape)).astype(jnp.bfloat16)
    in_grad = scatter_sum_by_all_to_all(in_part, "col", n_col).astype(jnp.bfloat16)

    def w_in_term(xs, p):
        return lax.dot_general(xs.reshape(-1, d_blk), p.reshape(-1, p.shape[-1]),
                               (((0,), (0,)), ((), ())), preferred_element_type=jnp.float32)

    w_in_grad = jnp.concatenate([
        w_in_term(inputs_all, pre_sc),
        w_in_term(x_rel, pre_a),
        w_in_term(jnp.swapaxes(x_rel, 0, 1), pre_b),
    ], axis=1).astype(jnp.bfloat16)
    return (in_grad, w_in_grad, w_out_grad)


def solution(mesh):
    in_specs = (P("col", "row"), P("col", "row"), P("row", "col"), P("row", "col"), P("col", "row"))
    out_specs = (P("col", "row"), P("row", "col"), P("col", "row"))
    return jax.shard_map(
        on_device, mesh=mesh, in_specs=in_specs, out_specs=out_specs, check_vma=False
    )
```

```python
import jax
import jax.numpy as jnp
from jax import lax
from jax.sharding import PartitionSpec as P


def gelu_parts(pre_act):
    value = pre_act.astype(jnp.float32)
    cumul = 0.5 * (1.0 + jax.scipy.special.erf(value * 0.7071067811865476))
    density = jnp.exp(-0.5 * value * value) * 0.3989422804014327
    return (value * cumul, cumul + value * density)


def gather_by_all_to_all(x, axis, n):
    rep = jnp.concatenate([x] * n, axis=0)
    return lax.all_to_all(rep, axis, 0, 0, tiled=True)


def scatter_sum_by_all_to_all(x, axis, n):
    got = lax.all_to_all(x, axis, 0, 0, tiled=True)
    got = got.reshape((n, x.shape[0] // n) + x.shape[1:])
    acc = got[0].astype(jnp.float32)
    for j in range(1, n):
        acc = acc + got[j].astype(jnp.float32)
    return acc


def gather_col_by_permutes(x, n_y):
    n_col = 2 * n_y
    me = lax.axis_index("col")
    pair = [(c, c ^ 1) for c in range(n_col)]
    other = lax.ppermute(x, "col", pair)
    core = me % 2
    both = jnp.where(core == 0, jnp.concatenate([x, other], 0), jnp.concatenate([other, x], 0))
    fwd = [(c, (c + 2) % n_col) for c in range(n_col)]
    bwd = [(c, (c - 2) % n_col) for c in range(n_col)]
    from_prev = lax.ppermute(both, "col", fwd)
    from_next = lax.ppermute(both, "col", bwd)
    blocks = [both, from_next]
    if n_y == 4:
        blocks.append(lax.ppermute(from_prev, "col", fwd))
    blocks.append(from_prev)
    rel = jnp.concatenate(blocks + blocks, axis=0)
    y = me // 2
    rows = both.shape[0] * n_y
    start = (n_y - y) % n_y * both.shape[0]
    return lax.dynamic_slice_in_dim(rel, start, rows, axis=0)


def ring_gather(x, fwd, bwd):
    from_prev = lax.ppermute(x, "row", fwd)
    from_next = lax.ppermute(x, "row", bwd)
    h = x.shape[0] // 2
    far = jnp.concatenate(
        [lax.ppermute(from_prev[:h], "row", fwd), lax.ppermute(from_next[h:], "row", bwd)], 0
    )
    return jnp.stack([x, from_next, far, from_prev])


def torus_gather(block, n_z, n_x, after):
    def perm(dz, dx):
        return [(z * n_x + x, ((z + dz) % n_z) * n_x + (x + dx) % n_x)
                for z in range(n_z) for x in range(n_x)]
    fx, bx, fz, bz = perm(0, 1), perm(0, -1), perm(1, 0), perm(-1, 0)
    w = block.shape[1] // 2
    a1 = ring_gather(block[:, :w], fx, bx)
    b1 = ring_gather(block[:, w:], fz, bz)
    a1, b1, after = lax.optimization_barrier((a1, b1, after))
    a = ring_gather(a1, fz, bz)
    b = ring_gather(b1, fx, bx)
    return a, b, after


def on_device(inputs, out_grad, pre_act, w_in, w_out):
    n_col = lax.psum(1, "col")
    value, slope = gelu_parts(pre_act)
    hidden_loc = value.astype(jnp.bfloat16)
    n_z, n_x = 4, 4
    grad_all = lax.all_gather(out_grad, "col", axis=0, tiled=True)
    hid_a, hid_b, grad_all = torus_gather(hidden_loc, n_z, n_x, grad_all)
    inputs_all = gather_by_all_to_all(inputs, "col", n_col)
    partial = lax.dot_general(
        grad_all, w_out, (((1,), (1,)), ((), ())), preferred_element_type=jnp.float32
    ).astype(jnp.bfloat16)
    total = lax.psum_scatter(partial, "row", scatter_dimension=0, tiled=True)
    me = lax.axis_index("row")
    grad4 = grad_all.reshape((n_z, n_x, -1, grad_all.shape[1]))
    grad_rel = jnp.roll(grad4, (-(me // n_x), -(me % n_x)), axis=(0, 1))
    width = hid_a.shape[-1]
    w_out_a = lax.dot_general(
        hid_a.reshape(-1, width), grad_rel.reshape(-1, grad_all.shape[1]),
        (((0,), (0,)), ((), ())), preferred_element_type=jnp.float32
    )
    w_out_b = lax.dot_general(
        hid_b.reshape(-1, width), jnp.swapaxes(grad_rel, 0, 1).reshape(-1, grad_all.shape[1]),
        (((0,), (0,)), ((), ())), preferred_element_type=jnp.float32
    )
    w_out_grad = jnp.concatenate([w_out_a, w_out_b], axis=0).astype(jnp.bfloat16)
    total, w_out_grad = lax.optimization_barrier((total, w_out_grad))
    pre_grad_loc = (total.astype(jnp.float32) * slope).astype(jnp.bfloat16)
    pre_grad = lax.all_gather(pre_grad_loc, "row", axis=0, tiled=True)
    in_part = lax.dot_general(
        pre_grad, w_in, (((1,), (1,)), ((), ())), preferred_element_type=jnp.float32
    ).astype(jnp.bfloat16)
    in_grad = scatter_sum_by_all_to_all(in_part, "col", n_col).astype(jnp.bfloat16)
    w_in_grad = lax.dot_general(
        inputs_all, pre_grad, (((0,), (0,)), ((), ())), preferred_element_type=jnp.float32
    ).astype(jnp.bfloat16)
    return (in_grad, w_in_grad, w_out_grad)


def solution(mesh):
    in_specs = (P("col", "row"), P("col", "row"), P("row", "col"), P("row", "col"), P("col", "row"))
    out_specs = (P("col", "row"), P("row", "col"), P("col", "row"))
    return jax.shard_map(
        on_device, mesh=mesh, in_specs=in_specs, out_specs=out_specs, check_vma=False
    )
```

```python
import jax
import jax.numpy as jnp
from jax import lax
from jax.sharding import PartitionSpec as P


def gelu_parts(pre_act):
    value = pre_act.astype(jnp.float32)
    cumul = 0.5 * (1.0 + jax.scipy.special.erf(value * 0.7071067811865476))
    density = jnp.exp(-0.5 * value * value) * 0.3989422804014327
    return (value * cumul, cumul + value * density)


def gather_by_all_to_all(x, axis, n):
    rep = jnp.concatenate([x] * n, axis=0)
    return lax.all_to_all(rep, axis, 0, 0, tiled=True)


def scatter_sum_by_all_to_all(x, axis, n):
    got = lax.all_to_all(x, axis, 0, 0, tiled=True)
    got = got.reshape((n, x.shape[0] // n) + x.shape[1:])
    acc = got[0].astype(jnp.float32)
    for j in range(1, n):
        acc = acc + got[j].astype(jnp.float32)
    return acc


def gather_col_by_permutes(x, n_y):
    n_col = 2 * n_y
    me = lax.axis_index("col")
    pair = [(c, c ^ 1) for c in range(n_col)]
    other = lax.ppermute(x, "col", pair)
    core = me % 2
    both = jnp.where(core == 0, jnp.concatenate([x, other], 0), jnp.concatenate([other, x], 0))
    fwd = [(c, (c + 2) % n_col) for c in range(n_col)]
    bwd = [(c, (c - 2) % n_col) for c in range(n_col)]
    from_prev = lax.ppermute(both, "col", fwd)
    from_next = lax.ppermute(both, "col", bwd)
    blocks = [both, from_next]
    if n_y == 4:
        blocks.append(lax.ppermute(from_prev, "col", fwd))
    blocks.append(from_prev)
    rel = jnp.concatenate(blocks + blocks, axis=0)
    y = me // 2
    rows = both.shape[0] * n_y
    start = (n_y - y) % n_y * both.shape[0]
    return lax.dynamic_slice_in_dim(rel, start, rows, axis=0)


def ring_gather(x, fwd, bwd, hold=None):
    from_prev = lax.ppermute(x, "row", fwd)
    from_next = lax.ppermute(x, "row", bwd)
    if hold is not None:
        from_prev, from_next, hold = lax.optimization_barrier((from_prev, from_next, hold))
    h = x.shape[0] // 2
    far = jnp.concatenate(
        [lax.ppermute(from_prev[:h], "row", fwd), lax.ppermute(from_next[h:], "row", bwd)], 0
    )
    return jnp.stack([x, from_next, far, from_prev]), hold


def torus_perms(n_z, n_x):
    def perm(dz, dx):
        return [(z * n_x + x, ((z + dz) % n_z) * n_x + (x + dx) % n_x)
                for z in range(n_z) for x in range(n_x)]
    return perm(0, 1), perm(0, -1), perm(1, 0), perm(-1, 0)


def on_device(inputs, out_grad, pre_act, w_in, w_out):
    n_col = lax.psum(1, "col")
    value, slope = gelu_parts(pre_act)
    hidden_loc = value.astype(jnp.bfloat16)
    n_z, n_x = 4, 4
    grad_all = lax.all_gather(out_grad, "col", axis=0, tiled=True)
    fx, bx, fz, bz = torus_perms(n_z, n_x)
    w = hidden_loc.shape[1] // 2
    a1, _ = ring_gather(hidden_loc[:, :w], fx, bx)
    b1, _ = ring_gather(hidden_loc[:, w:], fz, bz)
    a1, b1, grad_all = lax.optimization_barrier((a1, b1, grad_all))
    inputs_all = gather_by_all_to_all(inputs, "col", n_col)
    partial = lax.dot_general(
        grad_all, w_out, (((1,), (1,)), ((), ())), preferred_element_type=jnp.float32
    ).astype(jnp.bfloat16)
    total = lax.psum_scatter(partial, "row", scatter_dimension=0, tiled=True)
    hid_a, total = ring_gather(a1, fz, bz, total)
    hid_b, total = ring_gather(b1, fx, bx, total)
    pre_grad_loc = (total.astype(jnp.float32) * slope).astype(jnp.bfloat16)
    pre_grad = lax.all_gather(pre_grad_loc, "row", axis=0, tiled=True)
    me = lax.axis_index("row")
    grad4 = grad_all.reshape((n_z, n_x, -1, grad_all.shape[1]))
    grad_rel = jnp.roll(grad4, (-(me // n_x), -(me % n_x)), axis=(0, 1))
    width = hid_a.shape[-1]
    w_out_a = lax.dot_general(
        hid_a.reshape(-1, width), grad_rel.reshape(-1, grad_all.shape[1]),
        (((0,), (0,)), ((), ())), preferred_element_type=jnp.float32
    )
    w_out_b = lax.dot_general(
        hid_b.reshape(-1, width), jnp.swapaxes(grad_rel, 0, 1).reshape(-1, grad_all.shape[1]),
        (((0,), (0,)), ((), ())), preferred_element_type=jnp.float32
    )
    w_out_grad = jnp.concatenate([w_out_a, w_out_b], axis=0).astype(jnp.bfloat16)
    pre_grad, w_out_grad = lax.optimization_barrier((pre_grad, w_out_grad))
    in_part = lax.dot_general(
        pre_grad, w_in, (((1,), (1,)), ((), ())), preferred_element_type=jnp.float32
    ).astype(jnp.bfloat16)
    in_grad = scatter_sum_by_all_to_all(in_part, "col", n_col).astype(jnp.bfloat16)
    w_in_grad = lax.dot_general(
        inputs_all, pre_grad, (((0,), (0,)), ((), ())), preferred_element_type=jnp.float32
    ).astype(jnp.bfloat16)
    return (in_grad, w_in_grad, w_out_grad)


def solution(mesh):
    in_specs = (P("col", "row"), P("col", "row"), P("row", "col"), P("row", "col"), P("col", "row"))
    out_specs = (P("col", "row"), P("row", "col"), P("col", "row"))
    return jax.shard_map(
        on_device, mesh=mesh, in_specs=in_specs, out_specs=out_specs, check_vma=False
    )
```

```python
import jax
import jax.numpy as jnp
from jax import lax
from jax.sharding import PartitionSpec as P


def gelu_parts(pre_act):
    value = pre_act.astype(jnp.float32)
    cumul = 0.5 * (1.0 + jax.scipy.special.erf(value * 0.7071067811865476))
    density = jnp.exp(-0.5 * value * value) * 0.3989422804014327
    return (value * cumul, cumul + value * density)


def gather_by_all_to_all(x, axis, n):
    rep = jnp.concatenate([x] * n, axis=0)
    return lax.all_to_all(rep, axis, 0, 0, tiled=True)


def scatter_sum_by_all_to_all(x, axis, n):
    got = lax.all_to_all(x, axis, 0, 0, tiled=True)
    got = got.reshape((n, x.shape[0] // n) + x.shape[1:])
    acc = got[0].astype(jnp.float32)
    for j in range(1, n):
        acc = acc + got[j].astype(jnp.float32)
    return acc


def gather_col_by_permutes(x, n_y):
    n_col = 2 * n_y
    me = lax.axis_index("col")
    pair = [(c, c ^ 1) for c in range(n_col)]
    other = lax.ppermute(x, "col", pair)
    core = me % 2
    both = jnp.where(core == 0, jnp.concatenate([x, other], 0), jnp.concatenate([other, x], 0))
    fwd = [(c, (c + 2) % n_col) for c in range(n_col)]
    bwd = [(c, (c - 2) % n_col) for c in range(n_col)]
    from_prev = lax.ppermute(both, "col", fwd)
    from_next = lax.ppermute(both, "col", bwd)
    blocks = [both, from_next]
    if n_y == 4:
        blocks.append(lax.ppermute(from_prev, "col", fwd))
    blocks.append(from_prev)
    rel = jnp.concatenate(blocks + blocks, axis=0)
    y = me // 2
    rows = both.shape[0] * n_y
    start = (n_y - y) % n_y * both.shape[0]
    return lax.dynamic_slice_in_dim(rel, start, rows, axis=0)


def ring_gather(x, fwd, bwd, hold=None):
    from_prev = lax.ppermute(x, "row", fwd)
    from_next = lax.ppermute(x, "row", bwd)
    if hold is not None:
        from_prev, from_next, hold = lax.optimization_barrier((from_prev, from_next, hold))
    h = x.shape[0] // 2
    far = jnp.concatenate(
        [lax.ppermute(from_prev[:h], "row", fwd), lax.ppermute(from_next[h:], "row", bwd)], 0
    )
    return jnp.stack([x, from_next, far, from_prev]), hold


def torus_perms(n_z, n_x):
    def perm(dz, dx):
        return [(z * n_x + x, ((z + dz) % n_z) * n_x + (x + dx) % n_x)
                for z in range(n_z) for x in range(n_x)]
    return perm(0, 1), perm(0, -1), perm(1, 0), perm(-1, 0)


def scatter_sum_col(x, n_y):
    n_col = 2 * n_y
    me = lax.axis_index("col")
    k, y = me % 2, me // 2
    blk = x.shape[0] // n_col
    x4 = x.reshape((n_y, 2, blk) + x.shape[1:])
    mine = lax.dynamic_index_in_dim(x4, k, axis=1, keepdims=False)
    other = lax.dynamic_index_in_dim(x4, 1 - k, axis=1, keepdims=False)
    got = lax.ppermute(other, "col", [(c, c ^ 1) for c in range(n_col)])
    pair = mine.astype(jnp.float32) + got.astype(jnp.float32)
    pair_b = pair.astype(jnp.bfloat16)
    acc = lax.dynamic_index_in_dim(pair, y, axis=0, keepdims=False)
    for d in range(1, n_y):
        send = lax.dynamic_index_in_dim(pair_b, (y + d) % n_y, axis=0, keepdims=False)
        recv = lax.ppermute(send, "col", [(c, (c + 2 * d) % n_col) for c in range(n_col)])
        acc = acc + recv.astype(jnp.float32)
    return acc


def on_device(inputs, out_grad, pre_act, w_in, w_out):
    n_col = lax.psum(1, "col")
    value, slope = gelu_parts(pre_act)
    hidden_loc = value.astype(jnp.bfloat16)
    n_z, n_x = 4, 4
    grad_all = lax.all_gather(out_grad, "col", axis=0, tiled=True)
    fx, bx, fz, bz = torus_perms(n_z, n_x)
    w = hidden_loc.shape[1] // 2
    a1, _ = ring_gather(hidden_loc[:, :w], fx, bx)
    b1, _ = ring_gather(hidden_loc[:, w:], fz, bz)
    a1, b1, grad_all = lax.optimization_barrier((a1, b1, grad_all))
    inputs_all = gather_by_all_to_all(inputs, "col", n_col)
    partial = lax.dot_general(
        grad_all, w_out, (((1,), (1,)), ((), ())), preferred_element_type=jnp.float32
    ).astype(jnp.bfloat16)
    total = lax.psum_scatter(partial, "row", scatter_dimension=0, tiled=True)
    hid_a, total = ring_gather(a1, fz, bz, total)
    hid_b, total = ring_gather(b1, fx, bx, total)
    pre_grad_loc = (total.astype(jnp.float32) * slope).astype(jnp.bfloat16)
    pre_grad = lax.all_gather(pre_grad_loc, "row", axis=0, tiled=True)
    me = lax.axis_index("row")
    grad4 = grad_all.reshape((n_z, n_x, -1, grad_all.shape[1]))
    grad_rel = jnp.roll(grad4, (-(me // n_x), -(me % n_x)), axis=(0, 1))
    width = hid_a.shape[-1]
    w_out_a = lax.dot_general(
        hid_a.reshape(-1, width), grad_rel.reshape(-1, grad_all.shape[1]),
        (((0,), (0,)), ((), ())), preferred_element_type=jnp.float32
    )
    w_out_b = lax.dot_general(
        hid_b.reshape(-1, width), jnp.swapaxes(grad_rel, 0, 1).reshape(-1, grad_all.shape[1]),
        (((0,), (0,)), ((), ())), preferred_element_type=jnp.float32
    )
    w_out_grad = jnp.concatenate([w_out_a, w_out_b], axis=0).astype(jnp.bfloat16)
    pre_grad, w_out_grad = lax.optimization_barrier((pre_grad, w_out_grad))
    in_part = lax.dot_general(
        pre_grad, w_in, (((1,), (1,)), ((), ())), preferred_element_type=jnp.float32
    ).astype(jnp.bfloat16)
    in_grad = scatter_sum_col(in_part, n_col // 2).astype(jnp.bfloat16)
    w_in_grad = lax.dot_general(
        inputs_all, pre_grad, (((0,), (0,)), ((), ())), preferred_element_type=jnp.float32
    ).astype(jnp.bfloat16)
    return (in_grad, w_in_grad, w_out_grad)


def solution(mesh):
    in_specs = (P("col", "row"), P("col", "row"), P("row", "col"), P("row", "col"), P("col", "row"))
    out_specs = (P("col", "row"), P("row", "col"), P("col", "row"))
    return jax.shard_map(
        on_device, mesh=mesh, in_specs=in_specs, out_specs=out_specs, check_vma=False
    )
```

```python
import jax
import jax.numpy as jnp
from jax import lax
from jax.sharding import PartitionSpec as P


def gelu_parts(pre_act):
    value = pre_act.astype(jnp.float32)
    cumul = 0.5 * (1.0 + jax.scipy.special.erf(value * 0.7071067811865476))
    density = jnp.exp(-0.5 * value * value) * 0.3989422804014327
    return (value * cumul, cumul + value * density)


def gather_by_all_to_all(x, axis, n):
    rep = jnp.concatenate([x] * n, axis=0)
    return lax.all_to_all(rep, axis, 0, 0, tiled=True)


def scatter_sum_by_all_to_all(x, axis, n):
    got = lax.all_to_all(x, axis, 0, 0, tiled=True)
    got = got.reshape((n, x.shape[0] // n) + x.shape[1:])
    acc = got[0].astype(jnp.float32)
    for j in range(1, n):
        acc = acc + got[j].astype(jnp.float32)
    return acc


def gather_col_by_permutes(x, n_y):
    n_col = 2 * n_y
    me = lax.axis_index("col")
    pair = [(c, c ^ 1) for c in range(n_col)]
    other = lax.ppermute(x, "col", pair)
    core = me % 2
    both = jnp.where(core == 0, jnp.concatenate([x, other], 0), jnp.concatenate([other, x], 0))
    fwd = [(c, (c + 2) % n_col) for c in range(n_col)]
    bwd = [(c, (c - 2) % n_col) for c in range(n_col)]
    from_prev = lax.ppermute(both, "col", fwd)
    from_next = lax.ppermute(both, "col", bwd)
    blocks = [both, from_next]
    if n_y == 4:
        blocks.append(lax.ppermute(from_prev, "col", fwd))
    blocks.append(from_prev)
    rel = jnp.concatenate(blocks + blocks, axis=0)
    y = me // 2
    rows = both.shape[0] * n_y
    start = (n_y - y) % n_y * both.shape[0]
    return lax.dynamic_slice_in_dim(rel, start, rows, axis=0)


def ring_gather(x, fwd, bwd, hold=None):
    from_prev = lax.ppermute(x, "row", fwd)
    from_next = lax.ppermute(x, "row", bwd)
    if hold is not None:
        from_prev, from_next, hold = lax.optimization_barrier((from_prev, from_next, hold))
    h = x.shape[0] // 2
    far = jnp.concatenate(
        [lax.ppermute(from_prev[:h], "row", fwd), lax.ppermute(from_next[h:], "row", bwd)], 0
    )
    return jnp.stack([x, from_next, far, from_prev]), hold


def torus_perms(n_z, n_x):
    def perm(dz, dx):
        return [(z * n_x + x, ((z + dz) % n_z) * n_x + (x + dx) % n_x)
                for z in range(n_z) for x in range(n_x)]
    return perm(0, 1), perm(0, -1), perm(1, 0), perm(-1, 0)


def scatter_sum_col(x, n_y):
    n_col = 2 * n_y
    me = lax.axis_index("col")
    k, y = me % 2, me // 2
    blk = x.shape[0] // n_col
    x4 = x.reshape((n_y, 2, blk) + x.shape[1:])
    mine = lax.dynamic_index_in_dim(x4, k, axis=1, keepdims=False)
    other = lax.dynamic_index_in_dim(x4, 1 - k, axis=1, keepdims=False)
    got = lax.ppermute(other, "col", [(c, c ^ 1) for c in range(n_col)])
    pair = mine.astype(jnp.float32) + got.astype(jnp.float32)
    pair_b = pair.astype(jnp.bfloat16)
    acc = lax.dynamic_index_in_dim(pair, y, axis=0, keepdims=False)
    for d in range(1, n_y):
        send = lax.dynamic_index_in_dim(pair_b, (y + d) % n_y, axis=0, keepdims=False)
        recv = lax.ppermute(send, "col", [(c, (c + 2 * d) % n_col) for c in range(n_col)])
        acc = acc + recv.astype(jnp.float32)
    return acc


def on_device(inputs, out_grad, pre_act, w_in, w_out):
    n_col = lax.psum(1, "col")
    value, slope = gelu_parts(pre_act)
    hidden_loc = value.astype(jnp.bfloat16)
    n_z, n_x = 4, 4
    grad_all = lax.all_gather(out_grad, "col", axis=0, tiled=True)
    fx, bx, fz, bz = torus_perms(n_z, n_x)
    w = hidden_loc.shape[1] // 2
    a1, _ = ring_gather(hidden_loc[:, :w], fx, bx)
    b1, _ = ring_gather(hidden_loc[:, w:], fz, bz)
    a1, b1, grad_all = lax.optimization_barrier((a1, b1, grad_all))
    inputs_all = gather_by_all_to_all(inputs, "col", n_col)
    partial = lax.dot_general(
        grad_all, w_out, (((1,), (1,)), ((), ())), preferred_element_type=jnp.float32
    ).astype(jnp.bfloat16)
    total = lax.psum_scatter(partial, "row", scatter_dimension=0, tiled=True)
    hid_a, total = ring_gather(a1, fz, bz, total)
    b1, total = lax.optimization_barrier((b1, total))
    hid_b, _ = ring_gather(b1, fx, bx)
    pre_grad_loc = (total.astype(jnp.float32) * slope).astype(jnp.bfloat16)
    pre_grad = lax.all_gather(pre_grad_loc, "row", axis=0, tiled=True)
    me = lax.axis_index("row")
    grad4 = grad_all.reshape((n_z, n_x, -1, grad_all.shape[1]))
    grad_rel = jnp.roll(grad4, (-(me // n_x), -(me % n_x)), axis=(0, 1))
    width = hid_a.shape[-1]
    w_out_a = lax.dot_general(
        hid_a.reshape(-1, width), grad_rel.reshape(-1, grad_all.shape[1]),
        (((0,), (0,)), ((), ())), preferred_element_type=jnp.float32
    )
    w_out_b = lax.dot_general(
        hid_b.reshape(-1, width), jnp.swapaxes(grad_rel, 0, 1).reshape(-1, grad_all.shape[1]),
        (((0,), (0,)), ((), ())), preferred_element_type=jnp.float32
    )
    w_out_grad = jnp.concatenate([w_out_a, w_out_b], axis=0).astype(jnp.bfloat16)
    pre_grad, w_out_grad = lax.optimization_barrier((pre_grad, w_out_grad))
    in_part = lax.dot_general(
        pre_grad, w_in, (((1,), (1,)), ((), ())), preferred_element_type=jnp.float32
    ).astype(jnp.bfloat16)
    in_grad = scatter_sum_col(in_part, n_col // 2).astype(jnp.bfloat16)
    w_in_grad = lax.dot_general(
        inputs_all, pre_grad, (((0,), (0,)), ((), ())), preferred_element_type=jnp.float32
    ).astype(jnp.bfloat16)
    return (in_grad, w_in_grad, w_out_grad)


def solution(mesh):
    in_specs = (P("col", "row"), P("col", "row"), P("row", "col"), P("row", "col"), P("col", "row"))
    out_specs = (P("col", "row"), P("row", "col"), P("col", "row"))
    return jax.shard_map(
        on_device, mesh=mesh, in_specs=in_specs, out_specs=out_specs, check_vma=False
    )
```

```python
import jax
import jax.numpy as jnp
from jax import lax
from jax.sharding import PartitionSpec as P


def gelu_parts(pre_act):
    value = pre_act.astype(jnp.float32)
    cumul = 0.5 * (1.0 + jax.scipy.special.erf(value * 0.7071067811865476))
    density = jnp.exp(-0.5 * value * value) * 0.3989422804014327
    return (value * cumul, cumul + value * density)


def gather_by_all_to_all(x, axis, n):
    rep = jnp.concatenate([x] * n, axis=0)
    return lax.all_to_all(rep, axis, 0, 0, tiled=True)


def scatter_sum_by_all_to_all(x, axis, n):
    got = lax.all_to_all(x, axis, 0, 0, tiled=True)
    got = got.reshape((n, x.shape[0] // n) + x.shape[1:])
    acc = got[0].astype(jnp.float32)
    for j in range(1, n):
        acc = acc + got[j].astype(jnp.float32)
    return acc


def gather_col_by_permutes(x, n_y):
    n_col = 2 * n_y
    me = lax.axis_index("col")
    pair = [(c, c ^ 1) for c in range(n_col)]
    other = lax.ppermute(x, "col", pair)
    core = me % 2
    both = jnp.where(core == 0, jnp.concatenate([x, other], 0), jnp.concatenate([other, x], 0))
    fwd = [(c, (c + 2) % n_col) for c in range(n_col)]
    bwd = [(c, (c - 2) % n_col) for c in range(n_col)]
    from_prev = lax.ppermute(both, "col", fwd)
    from_next = lax.ppermute(both, "col", bwd)
    blocks = [both, from_next]
    if n_y == 4:
        blocks.append(lax.ppermute(from_prev, "col", fwd))
    blocks.append(from_prev)
    rel = jnp.concatenate(blocks + blocks, axis=0)
    y = me // 2
    rows = both.shape[0] * n_y
    start = (n_y - y) % n_y * both.shape[0]
    return lax.dynamic_slice_in_dim(rel, start, rows, axis=0)


def ring_gather(x, fwd, bwd, hold=None):
    from_prev = lax.ppermute(x, "row", fwd)
    from_next = lax.ppermute(x, "row", bwd)
    if hold is not None:
        from_prev, from_next, hold = lax.optimization_barrier((from_prev, from_next, hold))
    h = x.shape[0] // 2
    far = jnp.concatenate(
        [lax.ppermute(from_prev[:h], "row", fwd), lax.ppermute(from_next[h:], "row", bwd)], 0
    )
    return jnp.stack([x, from_next, far, from_prev]), hold


def torus_perms(n_z, n_x):
    def perm(dz, dx):
        return [(z * n_x + x, ((z + dz) % n_z) * n_x + (x + dx) % n_x)
                for z in range(n_z) for x in range(n_x)]
    return perm(0, 1), perm(0, -1), perm(1, 0), perm(-1, 0)


def in_grad_col(pre_grad, w_in, n_y):
    n_col = 2 * n_y
    me = lax.axis_index("col")
    k, y = me % 2, me // 2
    blk = pre_grad.shape[0] // n_col
    p4 = pre_grad.reshape((n_y, 2, blk) + pre_grad.shape[1:])

    def rows_for(core):
        p = lax.dynamic_index_in_dim(p4, core, axis=1, keepdims=False)
        return lax.dot_general(p, w_in, (((2,), (1,)), ((), ())),
                               preferred_element_type=jnp.float32)

    other = rows_for(1 - k).astype(jnp.bfloat16)
    got = lax.ppermute(other, "col", [(c, c ^ 1) for c in range(n_col)])
    mine = lax.optimization_barrier(rows_for(k).astype(jnp.bfloat16))
    pair = mine.astype(jnp.float32) + got.astype(jnp.float32)
    pair_b = pair.astype(jnp.bfloat16)
    acc = lax.dynamic_index_in_dim(pair, y, axis=0, keepdims=False)
    for d in range(1, n_y):
        send = lax.dynamic_index_in_dim(pair_b, (y + d) % n_y, axis=0, keepdims=False)
        recv = lax.ppermute(send, "col", [(c, (c + 2 * d) % n_col) for c in range(n_col)])
        acc = acc + recv.astype(jnp.float32)
    return acc


def on_device(inputs, out_grad, pre_act, w_in, w_out):
    n_col = lax.psum(1, "col")
    value, slope = gelu_parts(pre_act)
    hidden_loc = value.astype(jnp.bfloat16)
    n_z, n_x = 4, 4
    grad_all = lax.all_gather(out_grad, "col", axis=0, tiled=True)
    fx, bx, fz, bz = torus_perms(n_z, n_x)
    w = hidden_loc.shape[1] // 2
    a1, _ = ring_gather(hidden_loc[:, :w], fx, bx)
    b1, _ = ring_gather(hidden_loc[:, w:], fz, bz)
    a1, b1, grad_all = lax.optimization_barrier((a1, b1, grad_all))
    inputs_all = gather_by_all_to_all(inputs, "col", n_col)
    partial = lax.dot_general(
        grad_all, w_out, (((1,), (1,)), ((), ())), preferred_element_type=jnp.float32
    ).astype(jnp.bfloat16)
    total = lax.psum_scatter(partial, "row", scatter_dimension=0, tiled=True)
    hid_a, total = ring_gather(a1, fz, bz, total)
    hid_b, total = ring_gather(b1, fx, bx, total)
    pre_grad_loc = (total.astype(jnp.float32) * slope).astype(jnp.bfloat16)
    pre_grad = lax.all_gather(pre_grad_loc, "row", axis=0, tiled=True)
    me = lax.axis_index("row")
    grad4 = grad_all.reshape((n_z, n_x, -1, grad_all.shape[1]))
    grad_rel = jnp.roll(grad4, (-(me // n_x), -(me % n_x)), axis=(0, 1))
    width = hid_a.shape[-1]
    w_out_a = lax.dot_general(
        hid_a.reshape(-1, width), grad_rel.reshape(-1, grad_all.shape[1]),
        (((0,), (0,)), ((), ())), preferred_element_type=jnp.float32
    )
    w_out_b = lax.dot_general(
        hid_b.reshape(-1, width), jnp.swapaxes(grad_rel, 0, 1).reshape(-1, grad_all.shape[1]),
        (((0,), (0,)), ((), ())), preferred_element_type=jnp.float32
    )
    w_out_grad = jnp.concatenate([w_out_a, w_out_b], axis=0).astype(jnp.bfloat16)
    pre_grad, w_out_grad = lax.optimization_barrier((pre_grad, w_out_grad))
    in_grad = in_grad_col(pre_grad, w_in, n_col // 2).astype(jnp.bfloat16)
    w_in_grad = lax.dot_general(
        inputs_all, pre_grad, (((0,), (0,)), ((), ())), preferred_element_type=jnp.float32
    ).astype(jnp.bfloat16)
    return (in_grad, w_in_grad, w_out_grad)


def solution(mesh):
    in_specs = (P("col", "row"), P("col", "row"), P("row", "col"), P("row", "col"), P("col", "row"))
    out_specs = (P("col", "row"), P("row", "col"), P("col", "row"))
    return jax.shard_map(
        on_device, mesh=mesh, in_specs=in_specs, out_specs=out_specs, check_vma=False
    )
```

```python
import jax
import jax.numpy as jnp
from jax import lax
from jax.sharding import PartitionSpec as P


def gelu_parts(pre_act):
    value = pre_act.astype(jnp.float32)
    cumul = 0.5 * (1.0 + jax.scipy.special.erf(value * 0.7071067811865476))
    density = jnp.exp(-0.5 * value * value) * 0.3989422804014327
    return (value * cumul, cumul + value * density)


def gather_by_all_to_all(x, axis, n):
    rep = jnp.concatenate([x] * n, axis=0)
    return lax.all_to_all(rep, axis, 0, 0, tiled=True)


def scatter_sum_by_all_to_all(x, axis, n):
    got = lax.all_to_all(x, axis, 0, 0, tiled=True)
    got = got.reshape((n, x.shape[0] // n) + x.shape[1:])
    acc = got[0].astype(jnp.float32)
    for j in range(1, n):
        acc = acc + got[j].astype(jnp.float32)
    return acc


def gather_col_by_permutes(x, n_y):
    n_col = 2 * n_y
    me = lax.axis_index("col")
    pair = [(c, c ^ 1) for c in range(n_col)]
    other = lax.ppermute(x, "col", pair)
    core = me % 2
    both = jnp.where(core == 0, jnp.concatenate([x, other], 0), jnp.concatenate([other, x], 0))
    fwd = [(c, (c + 2) % n_col) for c in range(n_col)]
    bwd = [(c, (c - 2) % n_col) for c in range(n_col)]
    from_prev = lax.ppermute(both, "col", fwd)
    from_next = lax.ppermute(both, "col", bwd)
    blocks = [both, from_next]
    if n_y == 4:
        blocks.append(lax.ppermute(from_prev, "col", fwd))
    blocks.append(from_prev)
    rel = jnp.concatenate(blocks + blocks, axis=0)
    y = me // 2
    rows = both.shape[0] * n_y
    start = (n_y - y) % n_y * both.shape[0]
    return lax.dynamic_slice_in_dim(rel, start, rows, axis=0)


def ring_gather(x, fwd, bwd, hold=None):
    from_prev = lax.ppermute(x, "row", fwd)
    from_next = lax.ppermute(x, "row", bwd)
    if hold is not None:
        from_prev, from_next, hold = lax.optimization_barrier((from_prev, from_next, hold))
    h = x.shape[0] // 2
    far = jnp.concatenate(
        [lax.ppermute(from_prev[:h], "row", fwd), lax.ppermute(from_next[h:], "row", bwd)], 0
    )
    return jnp.stack([x, from_next, far, from_prev]), hold


def torus_perms(n_z, n_x):
    def perm(dz, dx):
        return [(z * n_x + x, ((z + dz) % n_z) * n_x + (x + dx) % n_x)
                for z in range(n_z) for x in range(n_x)]
    return perm(0, 1), perm(0, -1), perm(1, 0), perm(-1, 0)


def scatter_sum_col(x, n_y):
    n_col = 2 * n_y
    me = lax.axis_index("col")
    k, y = me % 2, me // 2
    blk = x.shape[0] // n_col
    x4 = x.reshape((n_y, 2, blk) + x.shape[1:])
    mine = lax.dynamic_index_in_dim(x4, k, axis=1, keepdims=False)
    other = lax.dynamic_index_in_dim(x4, 1 - k, axis=1, keepdims=False)
    got = lax.ppermute(other, "col", [(c, c ^ 1) for c in range(n_col)])
    pair = mine.astype(jnp.float32) + got.astype(jnp.float32)
    pair_b = pair.astype(jnp.bfloat16)
    acc = lax.dynamic_index_in_dim(pair, y, axis=0, keepdims=False)
    for d in range(1, n_y):
        send = lax.dynamic_index_in_dim(pair_b, (y + d) % n_y, axis=0, keepdims=False)
        recv = lax.ppermute(send, "col", [(c, (c + 2 * d) % n_col) for c in range(n_col)])
        acc = acc + recv.astype(jnp.float32)
    return acc


def gather_col_pair_ring(x, n_y):
    n_col = 2 * n_y
    me = lax.axis_index("col")
    k, y = me % 2, me // 2
    other = lax.ppermute(x, "col", [(c, c ^ 1) for c in range(n_col)])
    both = jnp.where(k == 0, jnp.concatenate([x, other], 0), jnp.concatenate([other, x], 0))
    recv = [lax.ppermute(both, "col", [(c, (c + 2 * d) % n_col) for c in range(n_col)])
            for d in range(1, n_y)]
    rel = jnp.stack([both] + recv[::-1])
    return jnp.roll(rel, y, axis=0).reshape((-1,) + x.shape[1:])


def on_device(inputs, out_grad, pre_act, w_in, w_out):
    n_col = lax.psum(1, "col")
    value, slope = gelu_parts(pre_act)
    hidden_loc = value.astype(jnp.bfloat16)
    n_z, n_x = 4, 4
    grad_all = gather_col_pair_ring(out_grad, n_col // 2)
    fx, bx, fz, bz = torus_perms(n_z, n_x)
    w = hidden_loc.shape[1] // 2
    a1, _ = ring_gather(hidden_loc[:, :w], fx, bx)
    b1, _ = ring_gather(hidden_loc[:, w:], fz, bz)
    a1, b1, grad_all = lax.optimization_barrier((a1, b1, grad_all))
    inputs_all = gather_by_all_to_all(inputs, "col", n_col)
    partial = lax.dot_general(
        grad_all, w_out, (((1,), (1,)), ((), ())), preferred_element_type=jnp.float32
    ).astype(jnp.bfloat16)
    total = lax.psum_scatter(partial, "row", scatter_dimension=0, tiled=True)
    hid_a, total = ring_gather(a1, fz, bz, total)
    hid_b, total = ring_gather(b1, fx, bx, total)
    pre_grad_loc = (total.astype(jnp.float32) * slope).astype(jnp.bfloat16)
    pre_grad = lax.all_gather(pre_grad_loc, "row", axis=0, tiled=True)
    me = lax.axis_index("row")
    grad4 = grad_all.reshape((n_z, n_x, -1, grad_all.shape[1]))
    grad_rel = jnp.roll(grad4, (-(me // n_x), -(me % n_x)), axis=(0, 1))
    width = hid_a.shape[-1]
    w_out_a = lax.dot_general(
        hid_a.reshape(-1, width), grad_rel.reshape(-1, grad_all.shape[1]),
        (((0,), (0,)), ((), ())), preferred_element_type=jnp.float32
    )
    w_out_b = lax.dot_general(
        hid_b.reshape(-1, width), jnp.swapaxes(grad_rel, 0, 1).reshape(-1, grad_all.shape[1]),
        (((0,), (0,)), ((), ())), preferred_element_type=jnp.float32
    )
    w_out_grad = jnp.concatenate([w_out_a, w_out_b], axis=0).astype(jnp.bfloat16)
    pre_grad, w_out_grad = lax.optimization_barrier((pre_grad, w_out_grad))
    in_part = lax.dot_general(
        pre_grad, w_in, (((1,), (1,)), ((), ())), preferred_element_type=jnp.float32
    ).astype(jnp.bfloat16)
    in_grad = scatter_sum_col(in_part, n_col // 2).astype(jnp.bfloat16)
    w_in_grad = lax.dot_general(
        inputs_all, pre_grad, (((0,), (0,)), ((), ())), preferred_element_type=jnp.float32
    ).astype(jnp.bfloat16)
    return (in_grad, w_in_grad, w_out_grad)


def solution(mesh):
    in_specs = (P("col", "row"), P("col", "row"), P("row", "col"), P("row", "col"), P("col", "row"))
    out_specs = (P("col", "row"), P("row", "col"), P("col", "row"))
    return jax.shard_map(
        on_device, mesh=mesh, in_specs=in_specs, out_specs=out_specs, check_vma=False
    )
```
